512 devices in a mesh: row: 64 (over x, y, core), col: 8 (over z).
Axes of the slice: x: 4, y: 8, z: 8, core: 2. Of those that a mesh axis runs over, the one named last changes fastest.
Arguments:
- grad_out: bfloat16 [2048, 12288], P('row', 'col'), may hold values from -3.5 to 3.5
- pre_act: bfloat16 [2048, 24576], P('col', 'row'), may hold values from -6 to 6
- down_weight: bfloat16 [24576, 12288], P('row', 'col'), may hold values from -0.0546875 to 0.0546875
Outputs:
- grad_pre: bfloat16 [2048, 24576], P('col', 'row')
- grad_weight: bfloat16 [24576, 12288], P('row', 'col')
The draws below stay inside these ranges and needn't reach their ends.
All inputs are finite; a program needn't handle non-finite values.
Results may differ from the reference program's by a relative error of at most 0.015.
Values may be sent and summed in bfloat16 or wider, within the bound.
No kernel may reach another device: no remote copies, remote signals or barrier semaphores. Data moves between devices by JAX's collectives and lax.ppermute only.
A program may use at most 64 MiB of HBM per device.

```python
import jax
import jax.numpy as jnp
from jax import lax

D = 12288
FF = 24576
TOKENS = 2048
N_COL = 8


def strengthened(array, own_key, source, target, shards_of, factor):
    owner, partner = [(jnp.arange(array.shape[position]) // (array.shape[position] // shards_of)).reshape([-1 if axis == position else 1 for axis in range(array.ndim)]) for position in (source, target)]
    chosen = jax.random.permutation(own_key, shards_of)[partner]
    strong = (owner == chosen) | (owner == (partner + shards_of // 2) % shards_of)
    return jnp.where(strong, factor * array, array)


def level_of(key, extent, cuts, smallest, top_value):
    factor_of, own = 1.0, jax.random.fold_in(key, 6)
    for axis_at, blocks in cuts:
        steps = jnp.exp(jax.random.uniform(jax.random.fold_in(own, axis_at), (blocks,), jnp.float32, smallest / len(cuts), top_value / len(cuts)))
        factor_of = factor_of * jnp.repeat(steps, extent[axis_at] // blocks).reshape([-1 if axis == axis_at else 1 for axis in range(len(extent))])
    return factor_of


def normal_values(rng, dims, spread, reach, shards=(), held_as=jnp.bfloat16):
    result = jax.random.normal(rng, dims, jnp.float32) * spread
    if len(shards) > 0:
        result = level_of(rng, dims, shards, -0.22, 0.18) * result
    return jnp.clip(result, min=-reach, max=reach).astype(held_as)


def noise_with(rng, extent, scale, reach, pieces, heavy, dtype=jnp.bfloat16):
    values = scale * jax.random.normal(rng, extent, jnp.float32)
    if pieces:
        values = values * level_of(rng, extent, pieces, -0.22, 0.18)
    return jnp.clip(strengthened(values, jax.random.fold_in(rng, 3), *heavy), -reach, reach).astype(dtype)


def setup_inputs(seed: int = 0) -> dict:
    seeds = jax.random.split(jax.random.key(seed), 4)
    grad_out = noise_with(seeds[0], (TOKENS, D), 0.2, 3.5, ((0, 64), (1, 8)), (1, 0, 64, 4.0))
    pre_act = normal_values(seeds[1], (TOKENS, FF), 1.5, 6.0, ((0, 8), (1, 64)))
    down_weight = normal_values(seeds[2], (FF, D), D ** -0.5, 0.0546875, ((0, 64), (1, 8)))
    return {"grad_out": grad_out, "pre_act": pre_act, "down_weight": down_weight}


coef = 0.7978845608
cubic = 0.044715

def gelu_fwd(x):
    return 0.5 * x * (1.0 + jnp.tanh(coef * (x + cubic * x * x * x)))

def gelu_grad(x):
    inner = coef * (x + cubic * x * x * x)
    tangent = jnp.tanh(inner)
    return 0.5 * (1.0 + tangent) + 0.5 * x * (1.0 - tangent * tangent) * coef * (1.0 + 3.0 * cubic * x * x)

def reference(grad_out, pre_act, down_weight):
    pre32 = pre_act.astype(jnp.float32)
    hidden = gelu_fwd(pre32).astype(jnp.bfloat16)
    blocks = 8
    width = FF // blocks
    hidden_blocks = jnp.transpose(hidden.reshape(TOKENS, blocks, width), (1, 0, 2))

    def one_block(piece):
        return lax.dot_general(piece, grad_out, (((0,), (0,)), ((), ())), preferred_element_type=jnp.float32).astype(jnp.bfloat16)
    grad_weight = lax.map(one_block, hidden_blocks).reshape(FF, D)
    feat_width = D // N_COL
    grad_blocks = jnp.transpose(grad_out.reshape(TOKENS, N_COL, feat_width), (1, 0, 2))
    weight_blocks = jnp.transpose(down_weight.reshape(FF, N_COL, feat_width), (1, 0, 2))

    def add_block(total, pair):
        partial_sum = lax.dot_general(pair[0], pair[1], (((1,), (1,)), ((), ())), preferred_element_type=jnp.float32)
        return (total + partial_sum.astype(jnp.bfloat16).astype(jnp.float32), None)
    start = jnp.zeros((TOKENS, FF), jnp.float32)
    grad_hidden, unused = lax.scan(add_block, start, (grad_blocks, weight_blocks))
    grad_pre = (grad_hidden * gelu_grad(pre32)).astype(jnp.bfloat16)
    return (grad_pre, grad_weight)
```

```python
import jax
import jax.numpy as jnp
from jax import lax
from jax.sharding import PartitionSpec as P

coef = 0.7978845608
cubic = 0.044715


def gelu_fwd(x):
    return 0.5 * x * (1.0 + jnp.tanh(coef * (x + cubic * x * x * x)))


def gelu_grad(x):
    inner = coef * (x + cubic * x * x * x)
    tangent = jnp.tanh(inner)
    return 0.5 * (1.0 + tangent) + 0.5 * x * (1.0 - tangent * tangent) * coef * (
        1.0 + 3.0 * cubic * x * x
    )


def body(grad_out, pre_act, down_weight):
    grad_all = lax.all_gather(grad_out, "row", axis=0, tiled=True)
    pre_all = lax.all_gather(pre_act, "col", axis=0, tiled=True)
    hidden = gelu_fwd(pre_all.astype(jnp.float32)).astype(jnp.bfloat16)
    grad_weight = lax.dot_general(
        hidden, grad_all, (((0,), (0,)), ((), ())), preferred_element_type=jnp.float32
    ).astype(jnp.bfloat16)
    partial_term = lax.dot_general(
        grad_all, down_weight, (((1,), (1,)), ((), ())), preferred_element_type=jnp.float32
    )
    grad_hidden = lax.psum_scatter(
        partial_term.astype(jnp.bfloat16), "col", scatter_dimension=0, tiled=True
    ).astype(jnp.float32)
    grad_pre = (grad_hidden * gelu_grad(pre_act.astype(jnp.float32))).astype(jnp.bfloat16)
    return (grad_pre, grad_weight)


def solution(mesh):
    in_specs = (P("row", "col"), P("col", "row"), P("row", "col"))
    out_specs = (P("col", "row"), P("row", "col"))
    return jax.shard_map(body, mesh=mesh, in_specs=in_specs, out_specs=out_specs, check_vma=False)
```

```python
import jax
import jax.numpy as jnp
import numpy as np
from jax import lax
from jax.sharding import Mesh
from jax.sharding import PartitionSpec as P

coef = 0.7978845608
cubic = 0.044715


def gelu_fwd(x):
    return 0.5 * x * (1.0 + jnp.tanh(coef * (x + cubic * x * x * x)))


def gelu_grad(x):
    inner = coef * (x + cubic * x * x * x)
    tangent = jnp.tanh(inner)
    return 0.5 * (1.0 + tangent) + 0.5 * x * (1.0 - tangent * tangent) * coef * (
        1.0 + 3.0 * cubic * x * x
    )


def ring_gather(block, axis, n):
    fwd = block
    bwd = block
    got = {0: block}
    for k in range(1, n // 2 + 1):
        fwd = lax.ppermute(fwd, axis, [(i, (i + 1) % n) for i in range(n)])
        got[(n - k) % n] = fwd
        if k < n - k:
            bwd = lax.ppermute(bwd, axis, [(i, (i - 1) % n) for i in range(n)])
            got[k] = bwd
    return jnp.stack([got[k] for k in range(n)])


def make_body(n_col, n_core):
    def body(grad_out, pre_act, down_weight):
        rc = lax.axis_index("rc")
        c = lax.axis_index("col")
        tok_blk = grad_out.shape[0]
        g_own = lax.all_gather(grad_out, "rp", axis=0, tiled=True)
        rel = ring_gather(pre_act, "col", n_col)
        g_own, rel = lax.optimization_barrier((g_own, rel))
        g_other = lax.ppermute(g_own, "rc", [(i, (i + 1) % n_core) for i in range(n_core)])
        both = jnp.concatenate([rel, rel], axis=0)
        pre_abs = lax.dynamic_slice_in_dim(both, (n_col - c) % n_col, n_col, 0)
        hidden = gelu_fwd(pre_abs.astype(jnp.float32)).astype(jnp.bfloat16)
        sub = pre_act.shape[0] // (tok_blk * n_core)
        h5 = hidden.reshape(n_col, sub, n_core, tok_blk, hidden.shape[-1])
        h_own = lax.dynamic_index_in_dim(h5, rc, 2, keepdims=False).reshape(-1, hidden.shape[-1])
        h_other = lax.dynamic_index_in_dim(h5, (rc + 1) % n_core, 2, keepdims=False).reshape(
            -1, hidden.shape[-1]
        )
        dn = (((0,), (0,)), ((), ()))
        gw = lax.dot_general(h_own, g_own, dn, preferred_element_type=jnp.float32)
        gw = gw + lax.dot_general(h_other, g_other, dn, preferred_element_type=jnp.float32)
        grad_weight = gw.astype(jnp.bfloat16)
        dn2 = (((1,), (1,)), ((), ()))
        p_own = lax.dot_general(g_own, down_weight, dn2, preferred_element_type=jnp.float32)
        p_other = lax.dot_general(g_other, down_weight, dn2, preferred_element_type=jnp.float32)
        stacked = jnp.stack([p_own, p_other]).astype(jnp.bfloat16)
        red = lax.psum_scatter(stacked, "col", scatter_dimension=1, tiled=True)
        red = red.astype(jnp.float32).reshape(n_core, sub, tok_blk, -1)
        first = jnp.where(rc == 0, red[0], red[1])
        second = jnp.where(rc == 0, red[1], red[0])
        grad_hidden = jnp.stack([first, second], axis=1).reshape(pre_act.shape)
        grad_pre = (grad_hidden * gelu_grad(pre_act.astype(jnp.float32))).astype(jnp.bfloat16)
        return (grad_pre, grad_weight)

    return body


def solution(mesh):
    devs = mesh.devices
    n_row, n_col = devs.shape
    chips = {tuple(getattr(d, "coords", (i,))) for i, d in enumerate(devs.flat)}
    n_core = max(1, devs.size // len(chips))
    split = Mesh(np.asarray(devs).reshape(n_row // n_core, n_core, n_col), ("rp", "rc", "col"))
    row = ("rp", "rc")
    in_specs = (P(row, "col"), P("col", row), P(row, "col"))
    out_specs = (P("col", row), P(row, "col"))
    return jax.shard_map(
        make_body(n_col, n_core), mesh=split, in_specs=in_specs, out_specs=out_specs, check_vma=False
    )
```

```python
import jax
import jax.numpy as jnp
import numpy as np
from jax import lax
from jax.sharding import Mesh
from jax.sharding import PartitionSpec as P

coef = 0.7978845608
cubic = 0.044715


def gelu_fwd(x):
    return 0.5 * x * (1.0 + jnp.tanh(coef * (x + cubic * x * x * x)))


def gelu_grad(x):
    inner = coef * (x + cubic * x * x * x)
    tangent = jnp.tanh(inner)
    return 0.5 * (1.0 + tangent) + 0.5 * x * (1.0 - tangent * tangent) * coef * (
        1.0 + 3.0 * cubic * x * x
    )


def ring_gather(block, axis, n):
    fwd = block
    bwd = block
    got = {0: block}
    for k in range(1, n // 2 + 1):
        fwd = lax.ppermute(fwd, axis, [(i, (i + 1) % n) for i in range(n)])
        got[(n - k) % n] = fwd
        if k < n - k:
            bwd = lax.ppermute(bwd, axis, [(i, (i - 1) % n) for i in range(n)])
            got[k] = bwd
    return jnp.stack([got[k] for k in range(n)])


def shift_pairs(n, s):
    return [(i, (i + s) % n) for i in range(n)]


def make_body(n_x, n_col, n_core):
    def body(grad_out, pre_act, down_weight):
        rc = lax.axis_index("rc")
        c = lax.axis_index("col")
        ix = lax.axis_index("rx")
        tok_blk, width = grad_out.shape
        rel_x = [grad_out] + [
            lax.ppermute(grad_out, "rx", shift_pairs(n_x, n_x - k)) for k in range(1, n_x)
        ]
        stack_x = jnp.stack(rel_x)
        twice_x = jnp.concatenate([stack_x, stack_x], axis=0)
        abs_x = lax.dynamic_slice_in_dim(twice_x, (n_x - ix) % n_x, n_x, 0)
        g_own = lax.all_gather(abs_x, "ry", axis=0, tiled=False)
        rel = ring_gather(pre_act, "col", n_col)
        g_own, rel = lax.optimization_barrier((g_own, rel))
        g_other = lax.ppermute(g_own, "rc", shift_pairs(n_core, 1))
        n_y = g_own.shape[0]
        both = jnp.concatenate([rel, rel], axis=0)
        pre_abs = lax.dynamic_slice_in_dim(both, (n_col - c) % n_col, n_col, 0)
        hidden = gelu_fwd(pre_abs.astype(jnp.float32)).astype(jnp.bfloat16)
        hid = hidden.shape[-1]
        h5 = hidden.reshape(n_x, n_y, n_core, tok_blk, hid)
        h5 = jnp.transpose(h5, (2, 1, 0, 3, 4))
        h_own = lax.dynamic_index_in_dim(h5, rc, 0, keepdims=False).reshape(-1, hid)
        h_other = lax.dynamic_index_in_dim(h5, (rc + 1) % n_core, 0, keepdims=False).reshape(-1, hid)
        go = g_own.reshape(-1, width)
        gt = g_other.reshape(-1, width)
        dn = (((0,), (0,)), ((), ()))
        gw = lax.dot_general(h_own, go, dn, preferred_element_type=jnp.float32)
        gw = gw + lax.dot_general(h_other, gt, dn, preferred_element_type=jnp.float32)
        grad_weight = gw.astype(jnp.bfloat16)
        dn2 = (((1,), (1,)), ((), ()))
        p_own = lax.dot_general(go, down_weight, dn2, preferred_element_type=jnp.float32)
        p_other = lax.dot_general(gt, down_weight, dn2, preferred_element_type=jnp.float32)
        stacked = jnp.stack([p_own, p_other]).astype(jnp.bfloat16)
        stacked = jnp.transpose(stacked.reshape(n_core, n_y, n_x, tok_blk, hid), (0, 2, 1, 3, 4))
        stacked = stacked.reshape(n_core, n_x * n_y * tok_blk, hid)
        red = lax.psum_scatter(stacked, "col", scatter_dimension=1, tiled=True)
        sub = pre_act.shape[0] // (tok_blk * n_core)
        red = red.astype(jnp.float32).reshape(n_core, sub, tok_blk, hid)
        first = jnp.where(rc == 0, red[0], red[1])
        second = jnp.where(rc == 0, red[1], red[0])
        grad_hidden = jnp.stack([first, second], axis=1).reshape(pre_act.shape)
        grad_pre = (grad_hidden * gelu_grad(pre_act.astype(jnp.float32))).astype(jnp.bfloat16)
        return (grad_pre, grad_weight)

    return body


def solution(mesh):
    devs = np.asarray(mesh.devices)
    n_row, n_col = devs.shape
    flat = list(devs.flat)
    chips = {tuple(getattr(d, "coords", (i,))) for i, d in enumerate(flat)}
    n_core = max(1, devs.size // len(chips))
    xs = {tuple(getattr(d, "coords", (i,)))[0] for i, d in enumerate(flat)}
    n_x = len(xs)
    split = Mesh(devs.reshape(n_x, n_row // (n_x * n_core), n_core, n_col), ("rx", "ry", "rc", "col"))
    row = ("rx", "ry", "rc")
    in_specs = (P(row, "col"), P("col", row), P(row, "col"))
    out_specs = (P("col", row), P(row, "col"))
    return jax.shard_map(
        make_body(n_x, n_col, n_core), mesh=split, in_specs=in_specs, out_specs=out_specs, check_vma=False
    )
```

```python
import jax
import jax.numpy as jnp
import numpy as np
from jax import lax
from jax.sharding import Mesh
from jax.sharding import PartitionSpec as P

coef = 0.7978845608
cubic = 0.044715


def gelu_fwd(x):
    return 0.5 * x * (1.0 + jnp.tanh(coef * (x + cubic * x * x * x)))


def gelu_grad(x):
    inner = coef * (x + cubic * x * x * x)
    tangent = jnp.tanh(inner)
    return 0.5 * (1.0 + tangent) + 0.5 * x * (1.0 - tangent * tangent) * coef * (
        1.0 + 3.0 * cubic * x * x
    )


def ring_gather(block, axis, n):
    fwd = block
    bwd = block
    got = {0: block}
    for k in range(1, n // 2 + 1):
        fwd = lax.ppermute(fwd, axis, [(i, (i + 1) % n) for i in range(n)])
        got[(n - k) % n] = fwd
        if k < n - k:
            bwd = lax.ppermute(bwd, axis, [(i, (i - 1) % n) for i in range(n)])
            got[k] = bwd
    return jnp.stack([got[k] for k in range(n)])


def shift_pairs(n, s):
    return [(i, (i + s) % n) for i in range(n)]


def make_body(n_x, n_col, n_core):
    def body(grad_out, pre_act, down_weight):
        rc = lax.axis_index("rc")
        c = lax.axis_index("col")
        tok_blk, width = grad_out.shape
        w_partner = lax.ppermute(down_weight, "rc", shift_pairs(n_core, 1))
        abs_x = lax.all_gather(grad_out, "rx", axis=0, tiled=False)
        g_own = lax.all_gather(abs_x, "ry", axis=0, tiled=False)
        rel = ring_gather(pre_act, "col", n_col)
        g_own, rel = lax.optimization_barrier((g_own, rel))
        g_other = lax.ppermute(g_own, "rc", shift_pairs(n_core, 1))
        n_y = g_own.shape[0]
        both = jnp.concatenate([rel, rel], axis=0)
        pre_abs = lax.dynamic_slice_in_dim(both, (n_col - c) % n_col, n_col, 0)
        hidden = gelu_fwd(pre_abs.astype(jnp.float32)).astype(jnp.bfloat16)
        hid = hidden.shape[-1]
        h5 = hidden.reshape(n_x, n_y, n_core, tok_blk, hid)
        h5 = jnp.transpose(h5, (2, 1, 0, 3, 4))
        h_own = lax.dynamic_index_in_dim(h5, rc, 0, keepdims=False).reshape(-1, hid)
        h_other = lax.dynamic_index_in_dim(h5, (rc + 1) % n_core, 0, keepdims=False).reshape(-1, hid)
        go = g_own.reshape(-1, width)
        gt = g_other.reshape(-1, width)
        dn = (((0,), (0,)), ((), ()))
        gw = lax.dot_general(h_own, go, dn, preferred_element_type=jnp.float32)
        gw = gw + lax.dot_general(h_other, gt, dn, preferred_element_type=jnp.float32)
        grad_weight = gw.astype(jnp.bfloat16)
        go_t = jnp.transpose(g_own, (1, 0, 2, 3)).reshape(-1, width)
        dn2 = (((1,), (1,)), ((), ()))
        p_mine = lax.dot_general(go_t, down_weight, dn2, preferred_element_type=jnp.float32)
        p_part = lax.dot_general(go_t, w_partner, dn2, preferred_element_type=jnp.float32)
        p_recv = lax.ppermute(p_part.astype(jnp.bfloat16), "rc", shift_pairs(n_core, 1))
        stacked = jnp.stack([p_mine.astype(jnp.bfloat16), p_recv])
        red = lax.psum_scatter(stacked, "col", scatter_dimension=1, tiled=True)
        sub = pre_act.shape[0] // (tok_blk * n_core)
        red = red.astype(jnp.float32).reshape(n_core, sub, tok_blk, hid)
        first = jnp.where(rc == 0, red[0], red[1])
        second = jnp.where(rc == 0, red[1], red[0])
        grad_hidden = jnp.stack([first, second], axis=1).reshape(pre_act.shape)
        grad_pre = (grad_hidden * gelu_grad(pre_act.astype(jnp.float32))).astype(jnp.bfloat16)
        return (grad_pre, grad_weight)

    return body


def solution(mesh):
    devs = np.asarray(mesh.devices)
    n_row, n_col = devs.shape
    flat = list(devs.flat)
    chips = {tuple(getattr(d, "coords", (i,))) for i, d in enumerate(flat)}
    n_core = max(1, devs.size // len(chips))
    xs = {tuple(getattr(d, "coords", (i,)))[0] for i, d in enumerate(flat)}
    n_x = len(xs)
    split = Mesh(devs.reshape(n_x, n_row // (n_x * n_core), n_core, n_col), ("rx", "ry", "rc", "col"))
    row = ("rx", "ry", "rc")
    in_specs = (P(row, "col"), P("col", row), P(row, "col"))
    out_specs = (P("col", row), P(row, "col"))
    return jax.shard_map(
        make_body(n_x, n_col, n_core), mesh=split, in_specs=in_specs, out_specs=out_specs, check_vma=False
    )
```

```python
import jax
import jax.numpy as jnp
import numpy as np
from jax import lax
from jax.sharding import Mesh
from jax.sharding import PartitionSpec as P

coef = 0.7978845608
cubic = 0.044715


def gelu_fwd(x):
    return 0.5 * x * (1.0 + jnp.tanh(coef * (x + cubic * x * x * x)))


def gelu_grad(x):
    inner = coef * (x + cubic * x * x * x)
    tangent = jnp.tanh(inner)
    return 0.5 * (1.0 + tangent) + 0.5 * x * (1.0 - tangent * tangent) * coef * (
        1.0 + 3.0 * cubic * x * x
    )


def ring_gather(block, axis, n):
    fwd = block
    bwd = block
    got = {0: block}
    for k in range(1, n // 2 + 1):
        fwd = lax.ppermute(fwd, axis, [(i, (i + 1) % n) for i in range(n)])
        got[(n - k) % n] = fwd
        if k < n - k:
            bwd = lax.ppermute(bwd, axis, [(i, (i - 1) % n) for i in range(n)])
            got[k] = bwd
    return jnp.stack([got[k] for k in range(n)])


def shift_pairs(n, s):
    return [(i, (i + s) % n) for i in range(n)]


def make_body(n_x, n_col, n_core):
    def body(grad_out, pre_act, down_weight):
        rc = lax.axis_index("rc")
        c = lax.axis_index("col")
        tok_blk, width = grad_out.shape
        w_partner = lax.ppermute(down_weight, "rc", shift_pairs(n_core, 1))
        abs_x = lax.all_gather(grad_out, "rx", axis=0, tiled=False)
        g_own = lax.all_gather(abs_x, "ry", axis=1, tiled=False)
        rel = ring_gather(pre_act, "col", n_col)
        g_own, rel = lax.optimization_barrier((g_own, rel))
        n_y = g_own.shape[1]
        both = jnp.concatenate([rel, rel], axis=0)
        pre_abs = lax.dynamic_slice_in_dim(both, (n_col - c) % n_col, n_col, 0)
        hidden = gelu_fwd(pre_abs.astype(jnp.float32)).astype(jnp.bfloat16)
        hid = hidden.shape[-1]
        h5 = hidden.reshape(n_x, n_y, n_core, tok_blk, hid)
        h5 = jnp.transpose(h5, (2, 0, 1, 3, 4))
        h_own = lax.dynamic_index_in_dim(h5, rc, 0, keepdims=False).reshape(-1, hid)
        h_other = lax.dynamic_index_in_dim(h5, (rc + 1) % n_core, 0, keepdims=False).reshape(-1, hid)
        go = g_own.reshape(-1, width)
        dn2 = (((1,), (1,)), ((), ()))
        p_mine = lax.dot_general(go, down_weight, dn2, preferred_element_type=jnp.float32)
        p_part = lax.dot_general(go, w_partner, dn2, preferred_element_type=jnp.float32)
        p_recv = lax.ppermute(p_part.astype(jnp.bfloat16), "rc", shift_pairs(n_core, 1))
        stacked = jnp.stack([p_mine.astype(jnp.bfloat16), p_recv])
        g_late, stacked = lax.optimization_barrier((g_own, stacked))
        g_other = lax.ppermute(g_late, "rc", shift_pairs(n_core, 1))
        red = lax.psum_scatter(stacked, "col", scatter_dimension=1, tiled=True)
        gt = g_other.reshape(-1, width)
        dn = (((0,), (0,)), ((), ()))
        gw = lax.dot_general(h_own, go, dn, preferred_element_type=jnp.float32)
        gw = gw + lax.dot_general(h_other, gt, dn, preferred_element_type=jnp.float32)
        grad_weight = gw.astype(jnp.bfloat16)
        sub = pre_act.shape[0] // (tok_blk * n_core)
        red = red.reshape(n_core, sub, tok_blk, hid)
        grad_weight, red = lax.optimization_barrier((grad_weight, red))
        first = lax.dynamic_index_in_dim(red, rc, 0, keepdims=False)
        second = lax.dynamic_index_in_dim(red, (rc + 1) % n_core, 0, keepdims=False)
        grad_hidden = jnp.stack([first, second], axis=1).reshape(pre_act.shape).astype(jnp.float32)
        grad_pre = (grad_hidden * gelu_grad(pre_act.astype(jnp.float32))).astype(jnp.bfloat16)
        return (grad_pre, grad_weight)

    return body


def solution(mesh):
    devs = np.asarray(mesh.devices)
    n_row, n_col = devs.shape
    flat = list(devs.flat)
    chips = {tuple(getattr(d, "coords", (i,))) for i, d in enumerate(flat)}
    n_core = max(1, devs.size // len(chips))
    xs = {tuple(getattr(d, "coords", (i,)))[0] for i, d in enumerate(flat)}
    n_x = len(xs)
    split = Mesh(devs.reshape(n_x, n_row // (n_x * n_core), n_core, n_col), ("rx", "ry", "rc", "col"))
    row = ("rx", "ry", "rc")
    in_specs = (P(row, "col"), P("col", row), P(row, "col"))
    out_specs = (P("col", row), P(row, "col"))
    return jax.shard_map(
        make_body(n_x, n_col, n_core), mesh=split, in_specs=in_specs, out_specs=out_specs, check_vma=False
    )
```

```python
import jax
import jax.numpy as jnp
import numpy as np
from jax import lax
from jax.sharding import Mesh
from jax.sharding import PartitionSpec as P

coef = 0.7978845608
cubic = 0.044715


def gelu_fwd(x):
    return 0.5 * x * (1.0 + jnp.tanh(coef * (x + cubic * x * x * x)))


def gelu_grad(x):
    inner = coef * (x + cubic * x * x * x)
    tangent = jnp.tanh(inner)
    return 0.5 * (1.0 + tangent) + 0.5 * x * (1.0 - tangent * tangent) * coef * (
        1.0 + 3.0 * cubic * x * x
    )


def ring_gather(block, axis, n):
    fwd = block
    bwd = block
    got = {0: block}
    for k in range(1, n // 2 + 1):
        fwd = lax.ppermute(fwd, axis, [(i, (i + 1) % n) for i in range(n)])
        got[(n - k) % n] = fwd
        if k < n - k:
            bwd = lax.ppermute(bwd, axis, [(i, (i - 1) % n) for i in range(n)])
            got[k] = bwd
    return jnp.stack([got[k] for k in range(n)])


def shift_pairs(n, s):
    return [(i, (i + s) % n) for i in range(n)]


def make_body(n_x, n_col, n_core):
    def body(grad_out, pre_act, down_weight):
        rc = lax.axis_index("rc")
        c = lax.axis_index("col")
        tok_blk, width = grad_out.shape
        w_partner = lax.ppermute(down_weight, "rc", shift_pairs(n_core, 1))
        w_both = jnp.concatenate([down_weight, w_partner], axis=0)
        abs_x = lax.all_gather(grad_out, "rx", axis=0, tiled=False)
        g_own = lax.all_gather(abs_x, "ry", axis=1, tiled=False)
        rel = ring_gather(pre_act, "col", n_col)
        g_own, rel = lax.optimization_barrier((g_own, rel))
        n_y = g_own.shape[1]
        both = jnp.concatenate([rel, rel], axis=0)
        pre_abs = lax.dynamic_slice_in_dim(both, (n_col - c) % n_col, n_col, 0)
        hidden = gelu_fwd(pre_abs.astype(jnp.float32)).astype(jnp.bfloat16)
        hid = hidden.shape[-1]
        h5 = hidden.reshape(n_x, n_y, n_core, tok_blk, hid)
        h5 = jnp.transpose(h5, (2, 0, 1, 3, 4))
        h_own = lax.dynamic_index_in_dim(h5, rc, 0, keepdims=False).reshape(-1, hid)
        h_other = lax.dynamic_index_in_dim(h5, (rc + 1) % n_core, 0, keepdims=False).reshape(-1, hid)
        go = g_own.reshape(-1, width)
        dn2 = (((1,), (1,)), ((), ()))
        p_both = lax.dot_general(go, w_both, dn2, preferred_element_type=jnp.float32)
        p_both = p_both.astype(jnp.bfloat16)
        g_late, p_both = lax.optimization_barrier((g_own, p_both))
        red = lax.psum_scatter(p_both, "col", scatter_dimension=0, tiled=True)
        g_other = lax.ppermute(g_late, "rc", shift_pairs(n_core, 1))
        gt = g_other.reshape(-1, width)
        dn = (((0,), (0,)), ((), ()))
        gw = lax.dot_general(h_own, go, dn, preferred_element_type=jnp.float32)
        gw = gw + lax.dot_general(h_other, gt, dn, preferred_element_type=jnp.float32)
        grad_weight = gw.astype(jnp.bfloat16)
        sub = pre_act.shape[0] // (tok_blk * n_core)
        grad_weight, red = lax.optimization_barrier((grad_weight, red))
        mine = red[:, :hid].reshape(sub, tok_blk, hid)
        theirs = lax.ppermute(red[:, hid:], "rc", shift_pairs(n_core, 1)).reshape(sub, tok_blk, hid)
        halves = jnp.stack([mine, theirs])
        first = lax.dynamic_index_in_dim(halves, rc, 0, keepdims=False)
        second = lax.dynamic_index_in_dim(halves, (rc + 1) % n_core, 0, keepdims=False)
        grad_hidden = jnp.stack([first, second], axis=1).reshape(pre_act.shape).astype(jnp.float32)
        grad_pre = (grad_hidden * gelu_grad(pre_act.astype(jnp.float32))).astype(jnp.bfloat16)
        return (grad_pre, grad_weight)

    return body


def solution(mesh):
    devs = np.asarray(mesh.devices)
    n_row, n_col = devs.shape
    flat = list(devs.flat)
    chips = {tuple(getattr(d, "coords", (i,))) for i, d in enumerate(flat)}
    n_core = max(1, devs.size // len(chips))
    xs = {tuple(getattr(d, "coords", (i,)))[0] for i, d in enumerate(flat)}
    n_x = len(xs)
    split = Mesh(devs.reshape(n_x, n_row // (n_x * n_core), n_core, n_col), ("rx", "ry", "rc", "col"))
    row = ("rx", "ry", "rc")
    in_specs = (P(row, "col"), P("col", row), P(row, "col"))
    out_specs = (P("col", row), P(row, "col"))
    return jax.shard_map(
        make_body(n_x, n_col, n_core), mesh=split, in_specs=in_specs, out_specs=out_specs, check_vma=False
    )
```

```python
import jax
import jax.numpy as jnp
import numpy as np
from jax import lax
from jax.sharding import Mesh
from jax.sharding import PartitionSpec as P

coef = 0.7978845608
cubic = 0.044715


def gelu_fwd(x):
    return 0.5 * x * (1.0 + jnp.tanh(coef * (x + cubic * x * x * x)))


def gelu_grad(x):
    inner = coef * (x + cubic * x * x * x)
    tangent = jnp.tanh(inner)
    return 0.5 * (1.0 + tangent) + 0.5 * x * (1.0 - tangent * tangent) * coef * (
        1.0 + 3.0 * cubic * x * x
    )


def ring_gather(block, axis, n):
    fwd = block
    bwd = block
    got = {0: block}
    for k in range(1, n // 2 + 1):
        fwd = lax.ppermute(fwd, axis, [(i, (i + 1) % n) for i in range(n)])
        got[(n - k) % n] = fwd
        if k < n - k:
            bwd = lax.ppermute(bwd, axis, [(i, (i - 1) % n) for i in range(n)])
            got[k] = bwd
    return [got[k] for k in range(n)]


def shift_pairs(n, s):
    return [(i, (i + s) % n) for i in range(n)]


def make_body(n_x, n_col, n_core):
    def body(grad_out, pre_act, down_weight):
        rc = lax.axis_index("rc")
        c = lax.axis_index("col")
        tok_blk, width = grad_out.shape
        w_partner = lax.ppermute(down_weight, "rc", shift_pairs(n_core, 1))
        abs_x = lax.all_gather(grad_out, "rx", axis=0, tiled=False)
        g_own = lax.all_gather(abs_x, "ry", axis=1, tiled=False)
        rel = ring_gather(pre_act, "col", n_col)
        n_y = g_own.shape[1]
        go = g_own.reshape(-1, width)
        dn2 = (((1,), (1,)), ((), ()))
        p_mine = lax.dot_general(go, down_weight, dn2, preferred_element_type=jnp.float32)
        p_part = lax.dot_general(go, w_partner, dn2, preferred_element_type=jnp.float32)
        p_both = jnp.stack([p_mine, p_part]).astype(jnp.bfloat16)
        g_late, rel, p_both = lax.optimization_barrier((g_own, rel, p_both))
        red = lax.psum_scatter(p_both, "col", scatter_dimension=1, tiled=True)
        g_other = lax.ppermute(g_late, "rc", shift_pairs(n_core, 1))
        rel = jnp.stack(rel)
        both = jnp.concatenate([rel, rel], axis=0)
        pre_abs = lax.dynamic_slice_in_dim(both, (n_col - c) % n_col, n_col, 0)
        hidden = gelu_fwd(pre_abs.astype(jnp.float32)).astype(jnp.bfloat16)
        hid = hidden.shape[-1]
        h5 = hidden.reshape(n_x, n_y, n_core, tok_blk, hid)
        h5 = jnp.transpose(h5, (2, 0, 1, 3, 4))
        h_own = lax.dynamic_index_in_dim(h5, rc, 0, keepdims=False).reshape(-1, hid)
        h_other = lax.dynamic_index_in_dim(h5, (rc + 1) % n_core, 0, keepdims=False).reshape(-1, hid)
        gt = g_other.reshape(-1, width)
        dn = (((0,), (0,)), ((), ()))
        gw = lax.dot_general(h_own, go, dn, preferred_element_type=jnp.float32)
        gw = gw + lax.dot_general(h_other, gt, dn, preferred_element_type=jnp.float32)
        grad_weight = gw.astype(jnp.bfloat16)
        sub = pre_act.shape[0] // (tok_blk * n_core)
        mine = red[0].reshape(sub, tok_blk, hid)
        theirs = lax.ppermute(red[1], "rc", shift_pairs(n_core, 1)).reshape(sub, tok_blk, hid)
        first = jnp.where(rc == 0, mine, theirs)
        second = jnp.where(rc == 0, theirs, mine)
        gg = gelu_grad(pre_act.astype(jnp.float32)).reshape(sub, n_core, tok_blk, hid)
        out0 = first.astype(jnp.float32) * gg[:, 0]
        out1 = second.astype(jnp.float32) * gg[:, 1]
        grad_pre = jnp.stack([out0, out1], axis=1).reshape(pre_act.shape).astype(jnp.bfloat16)
        return (grad_pre, grad_weight)

    return body


def solution(mesh):
    devs = np.asarray(mesh.devices)
    n_row, n_col = devs.shape
    flat = list(devs.flat)
    chips = {tuple(getattr(d, "coords", (i,))) for i, d in enumerate(flat)}
    n_core = max(1, devs.size // len(chips))
    xs = {tuple(getattr(d, "coords", (i,)))[0] for i, d in enumerate(flat)}
    n_x = len(xs)
    split = Mesh(devs.reshape(n_x, n_row // (n_x * n_core), n_core, n_col), ("rx", "ry", "rc", "col"))
    row = ("rx", "ry", "rc")
    in_specs = (P(row, "col"), P("col", row), P(row, "col"))
    out_specs = (P("col", row), P(row, "col"))
    return jax.shard_map(
        make_body(n_x, n_col, n_core), mesh=split, in_specs=in_specs, out_specs=out_specs, check_vma=False
    )
```

```python
import jax
import jax.numpy as jnp
import numpy as np
from jax import lax
from jax.sharding import Mesh
from jax.sharding import PartitionSpec as P

coef = 0.7978845608
cubic = 0.044715


def gelu_fwd(x):
    return 0.5 * x * (1.0 + jnp.tanh(coef * (x + cubic * x * x * x)))


def gelu_grad(x):
    inner = coef * (x + cubic * x * x * x)
    tangent = jnp.tanh(inner)
    return 0.5 * (1.0 + tangent) + 0.5 * x * (1.0 - tangent * tangent) * coef * (
        1.0 + 3.0 * cubic * x * x
    )


def ring_gather(block, axis, n):
    fwd = block
    bwd = block
    got = {0: block}
    for k in range(1, n // 2 + 1):
        fwd = lax.ppermute(fwd, axis, [(i, (i + 1) % n) for i in range(n)])
        got[(n - k) % n] = fwd
        if k < n - k:
            bwd = lax.ppermute(bwd, axis, [(i, (i - 1) % n) for i in range(n)])
            got[k] = bwd
    return [got[k] for k in range(n)]


def shift_pairs(n, s):
    return [(i, (i + s) % n) for i in range(n)]


def make_body(n_x, n_col, n_core):
    def body(grad_out, pre_act, down_weight):
        rc = lax.axis_index("rc")
        c = lax.axis_index("col")
        tok_blk, width = grad_out.shape
        w_partner = lax.ppermute(down_weight, "rc", shift_pairs(n_core, 1))
        abs_x = lax.all_gather(grad_out, "rx", axis=0, tiled=False)
        g_own = lax.all_gather(abs_x, "ry", axis=1, tiled=False)
        rel = ring_gather(pre_act, "col", n_col)
        n_y = g_own.shape[1]
        go = g_own.reshape(-1, width)
        dn2 = (((1,), (1,)), ((), ()))
        p_mine = lax.dot_general(go, down_weight, dn2, preferred_element_type=jnp.float32)
        p_part = lax.dot_general(go, w_partner, dn2, preferred_element_type=jnp.float32)
        p_both = jnp.stack([p_mine, p_part]).astype(jnp.bfloat16)
        g_late, rel, p_both = lax.optimization_barrier((g_own, rel, p_both))
        red = lax.psum_scatter(p_both, "col", scatter_dimension=1, tiled=True)
        g_other = lax.ppermute(g_late, "rc", shift_pairs(n_core, 1))
        rel = jnp.stack(rel)
        both = jnp.concatenate([rel, rel], axis=0)
        pre_abs = lax.dynamic_slice_in_dim(both, (n_col - c) % n_col, n_col, 0)
        hidden = gelu_fwd(pre_abs.astype(jnp.float32)).astype(jnp.bfloat16)
        hid = hidden.shape[-1]
        h5 = hidden.reshape(n_x, n_y, n_core, tok_blk, hid)
        h5 = jnp.transpose(h5, (2, 0, 1, 3, 4))
        h_own = lax.dynamic_index_in_dim(h5, rc, 0, keepdims=False).reshape(-1, hid)
        h_other = lax.dynamic_index_in_dim(h5, (rc + 1) % n_core, 0, keepdims=False).reshape(-1, hid)
        gt = g_other.reshape(-1, width)
        dn = (((0,), (0,)), ((), ()))
        gw = lax.dot_general(h_own, go, dn, preferred_element_type=jnp.float32)
        gw = gw + lax.dot_general(h_other, gt, dn, preferred_element_type=jnp.float32)
        grad_weight = gw.astype(jnp.bfloat16)
        sub = pre_act.shape[0] // (tok_blk * n_core)
        grad_weight, red = lax.optimization_barrier((grad_weight, red))
        mine = red[0].reshape(sub, tok_blk, hid)
        theirs = lax.ppermute(red[1], "rc", shift_pairs(n_core, 1)).reshape(sub, tok_blk, hid)
        first = jnp.where(rc == 0, mine, theirs)
        second = jnp.where(rc == 0, theirs, mine)
        gg = gelu_grad(pre_act.astype(jnp.float32)).reshape(sub, n_core, tok_blk, hid)
        out0 = first.astype(jnp.float32) * gg[:, 0]
        out1 = second.astype(jnp.float32) * gg[:, 1]
        grad_pre = jnp.stack([out0, out1], axis=1).reshape(pre_act.shape).astype(jnp.bfloat16)
        return (grad_pre, grad_weight)

    return body


def solution(mesh):
    devs = np.asarray(mesh.devices)
    n_row, n_col = devs.shape
    flat = list(devs.flat)
    chips = {tuple(getattr(d, "coords", (i,))) for i, d in enumerate(flat)}
    n_core = max(1, devs.size // len(chips))
    xs = {tuple(getattr(d, "coords", (i,)))[0] for i, d in enumerate(flat)}
    n_x = len(xs)
    split = Mesh(devs.reshape(n_x, n_row // (n_x * n_core), n_core, n_col), ("rx", "ry", "rc", "col"))
    row = ("rx", "ry", "rc")
    in_specs = (P(row, "col"), P("col", row), P(row, "col"))
    out_specs = (P("col", row), P(row, "col"))
    return jax.shard_map(
        make_body(n_x, n_col, n_core), mesh=split, in_specs=in_specs, out_specs=out_specs, check_vma=False
    )
```

```python
import jax
import jax.numpy as jnp
import numpy as np
from jax import lax
from jax.sharding import Mesh
from jax.sharding import PartitionSpec as P

coef = 0.7978845608
cubic = 0.044715


def gelu_fwd(x):
    return 0.5 * x * (1.0 + jnp.tanh(coef * (x + cubic * x * x * x)))


def gelu_grad(x):
    inner = coef * (x + cubic * x * x * x)
    tangent = jnp.tanh(inner)
    return 0.5 * (1.0 + tangent) + 0.5 * x * (1.0 - tangent * tangent) * coef * (
        1.0 + 3.0 * cubic * x * x
    )


def ring_gather(block, axis, n):
    fwd = block
    bwd = block
    got = {0: block}
    for k in range(1, n // 2 + 1):
        fwd = lax.ppermute(fwd, axis, [(i, (i + 1) % n) for i in range(n)])
        got[(n - k) % n] = fwd
        if k < n - k:
            bwd = lax.ppermute(bwd, axis, [(i, (i - 1) % n) for i in range(n)])
            got[k] = bwd
    return [got[k] for k in range(n)]


def shift_pairs(n, s):
    return [(i, (i + s) % n) for i in range(n)]


def make_body(n_x, n_y, n_col, n_core):
    def body(grad_out, pre_act, down_weight):
        rc = lax.axis_index("rc")
        c = lax.axis_index("col")
        tok_blk, width = grad_out.shape
        w_partner = lax.ppermute(down_weight, "rc", shift_pairs(n_core, 1))
        abs_x = lax.all_gather(grad_out, "rx", axis=0, tiled=False)
        rel_y = ring_gather(abs_x, "ry", n_y)
        iy = lax.axis_index("ry")
        stack_y = jnp.stack(rel_y, axis=1)
        twice_y = jnp.concatenate([stack_y, stack_y], axis=1)
        g_own = lax.dynamic_slice_in_dim(twice_y, (n_y - iy) % n_y, n_y, 1)
        rel = ring_gather(pre_act, "col", n_col)
        go = g_own.reshape(-1, width)
        dn2 = (((1,), (1,)), ((), ()))
        p_mine = lax.dot_general(go, down_weight, dn2, preferred_element_type=jnp.float32)
        p_part = lax.dot_general(go, w_partner, dn2, preferred_element_type=jnp.float32)
        p_both = jnp.stack([p_mine, p_part]).astype(jnp.bfloat16)
        g_late, rel, p_both = lax.optimization_barrier((g_own, rel, p_both))
        blocks = p_both.reshape(n_core, n_col, -1, down_weight.shape[0])
        twice_b = jnp.concatenate([blocks, blocks], axis=1)
        rel_b = lax.dynamic_slice_in_dim(twice_b, c, n_col, 1)
        acc = rel_b[:, 0].astype(jnp.float32)
        for k in range(1, n_col):
            acc = acc + lax.ppermute(rel_b[:, k], "col", shift_pairs(n_col, k)).astype(jnp.float32)
        red = acc.astype(jnp.bfloat16)
        g_other = lax.ppermute(g_late, "rc", shift_pairs(n_core, 1))
        rel = jnp.stack(rel)
        both = jnp.concatenate([rel, rel], axis=0)
        pre_abs = lax.dynamic_slice_in_dim(both, (n_col - c) % n_col, n_col, 0)
        hidden = gelu_fwd(pre_abs.astype(jnp.float32)).astype(jnp.bfloat16)
        hid = hidden.shape[-1]
        h5 = hidden.reshape(n_x, n_y, n_core, tok_blk, hid)
        h5 = jnp.transpose(h5, (2, 0, 1, 3, 4))
        h_own = lax.dynamic_index_in_dim(h5, rc, 0, keepdims=False).reshape(-1, hid)
        h_other = lax.dynamic_index_in_dim(h5, (rc + 1) % n_core, 0, keepdims=False).reshape(-1, hid)
        gt = g_other.reshape(-1, width)
        dn = (((0,), (0,)), ((), ()))
        gw = lax.dot_general(h_own, go, dn, preferred_element_type=jnp.float32)
        gw = gw + lax.dot_general(h_other, gt, dn, preferred_element_type=jnp.float32)
        grad_weight = gw.astype(jnp.bfloat16)
        sub = pre_act.shape[0] // (tok_blk * n_core)
        grad_weight, red = lax.optimization_barrier((grad_weight, red))
        mine = red[0].reshape(sub, tok_blk, hid)
        theirs = lax.ppermute(red[1], "rc", shift_pairs(n_core, 1)).reshape(sub, tok_blk, hid)
        first = jnp.where(rc == 0, mine, theirs)
        second = jnp.where(rc == 0, theirs, mine)
        gg = gelu_grad(pre_act.astype(jnp.float32)).reshape(sub, n_core, tok_blk, hid)
        out0 = first.astype(jnp.float32) * gg[:, 0]
        out1 = second.astype(jnp.float32) * gg[:, 1]
        grad_pre = jnp.stack([out0, out1], axis=1).reshape(pre_act.shape).astype(jnp.bfloat16)
        return (grad_pre, grad_weight)

    return body


def solution(mesh):
    devs = np.asarray(mesh.devices)
    n_row, n_col = devs.shape
    flat = list(devs.flat)
    chips = {tuple(getattr(d, "coords", (i,))) for i, d in enumerate(flat)}
    n_core = max(1, devs.size // len(chips))
    xs = {tuple(getattr(d, "coords", (i,)))[0] for i, d in enumerate(flat)}
    n_x = len(xs)
    split = Mesh(devs.reshape(n_x, n_row // (n_x * n_core), n_core, n_col), ("rx", "ry", "rc", "col"))
    row = ("rx", "ry", "rc")
    in_specs = (P(row, "col"), P("col", row), P(row, "col"))
    out_specs = (P("col", row), P(row, "col"))
    return jax.shard_map(
        make_body(n_x, n_row // (n_x * n_core), n_col, n_core), mesh=split, in_specs=in_specs, out_specs=out_specs, check_vma=False
    )
```

```python
import jax
import jax.numpy as jnp
import numpy as np
from jax import lax
from jax.sharding import Mesh
from jax.sharding import PartitionSpec as P

coef = 0.7978845608
cubic = 0.044715


def gelu_fwd(x):
    return 0.5 * x * (1.0 + jnp.tanh(coef * (x + cubic * x * x * x)))


def gelu_grad(x):
    inner = coef * (x + cubic * x * x * x)
    tangent = jnp.tanh(inner)
    return 0.5 * (1.0 + tangent) + 0.5 * x * (1.0 - tangent * tangent) * coef * (
        1.0 + 3.0 * cubic * x * x
    )


def ring_gather(block, axis, n):
    fwd = block
    bwd = block
    got = {0: block}
    for k in range(1, n // 2 + 1):
        fwd = lax.ppermute(fwd, axis, [(i, (i + 1) % n) for i in range(n)])
        got[(n - k) % n] = fwd
        if k < n - k:
            bwd = lax.ppermute(bwd, axis, [(i, (i - 1) % n) for i in range(n)])
            got[k] = bwd
    return [got[k] for k in range(n)]


def shift_pairs(n, s):
    return [(i, (i + s) % n) for i in range(n)]


def make_body(n_x, n_col, n_core):
    def body(grad_out, pre_act, down_weight):
        rc = lax.axis_index("rc")
        c = lax.axis_index("col")
        tok_blk, width = grad_out.shape
        w_partner = lax.ppermute(down_weight, "rc", shift_pairs(n_core, 1))
        abs_x = lax.all_gather(grad_out, "rx", axis=0, tiled=False)
        g_own = lax.all_gather(abs_x, "ry", axis=1, tiled=False)
        rel = ring_gather(pre_act, "col", n_col)
        n_y = g_own.shape[1]
        go = g_own.reshape(-1, width)
        dn2 = (((1,), (1,)), ((), ()))
        p_mine = lax.dot_general(go, down_weight, dn2, preferred_element_type=jnp.float32)
        p_part = lax.dot_general(go, w_partner, dn2, preferred_element_type=jnp.float32)
        p_both = jnp.stack([p_mine, p_part]).astype(jnp.bfloat16)
        g_late, rel, p_both = lax.optimization_barrier((g_own, rel, p_both))
        red = lax.psum_scatter(p_both, "col", scatter_dimension=1, tiled=True)
        g_other = lax.ppermute(g_late, "rc", shift_pairs(n_core, 1))
        rel = jnp.stack(rel)
        both = jnp.concatenate([rel, rel], axis=0)
        pre_abs = lax.dynamic_slice_in_dim(both, (n_col - c) % n_col, n_col, 0)
        hidden = gelu_fwd(pre_abs.astype(jnp.float32)).astype(jnp.bfloat16)
        hid = hidden.shape[-1]
        h5 = hidden.reshape(n_x, n_y, n_core, tok_blk, hid)
        h5 = jnp.transpose(h5, (2, 0, 1, 3, 4))
        h_own = lax.dynamic_index_in_dim(h5, rc, 0, keepdims=False).reshape(-1, hid)
        h_other = lax.dynamic_index_in_dim(h5, (rc + 1) % n_core, 0, keepdims=False).reshape(-1, hid)
        gt = g_other.reshape(-1, width)
        dn = (((0,), (0,)), ((), ()))
        gw = lax.dot_general(h_own, go, dn, preferred_element_type=jnp.float32)
        gw = gw + lax.dot_general(h_other, gt, dn, preferred_element_type=jnp.float32)
        grad_weight = gw.astype(jnp.bfloat16)
        sub = pre_act.shape[0] // (tok_blk * n_core)
        grad_weight, red = lax.optimization_barrier((grad_weight, red))
        got = lax.ppermute(red, "rc", shift_pairs(n_core, 1))
        mine = red[0].reshape(sub, 1, tok_blk, hid)
        theirs = got[1].reshape(sub, 1, tok_blk, hid)
        slot = lax.broadcasted_iota(jnp.int32, (sub, n_core, tok_blk, hid), 1)
        gh = jnp.where(slot == rc, mine, theirs).astype(jnp.float32)
        gg = gelu_grad(pre_act.astype(jnp.float32)).reshape(sub, n_core, tok_blk, hid)
        grad_pre = (gh * gg).reshape(pre_act.shape).astype(jnp.bfloat16)
        return (grad_pre, grad_weight)

    return body


def solution(mesh):
    devs = np.asarray(mesh.devices)
    n_row, n_col = devs.shape
    flat = list(devs.flat)
    chips = {tuple(getattr(d, "coords", (i,))) for i, d in enumerate(flat)}
    n_core = max(1, devs.size // len(chips))
    xs = {tuple(getattr(d, "coords", (i,)))[0] for i, d in enumerate(flat)}
    n_x = len(xs)
    split = Mesh(devs.reshape(n_x, n_row // (n_x * n_core), n_core, n_col), ("rx", "ry", "rc", "col"))
    row = ("rx", "ry", "rc")
    in_specs = (P(row, "col"), P("col", row), P(row, "col"))
    out_specs = (P("col", row), P(row, "col"))
    return jax.shard_map(
        make_body(n_x, n_col, n_core), mesh=split, in_specs=in_specs, out_specs=out_specs, check_vma=False
    )
```

```python
import jax
import jax.numpy as jnp
import numpy as np
from jax import lax
from jax.sharding import Mesh
from jax.sharding import PartitionSpec as P

coef = 0.7978845608
cubic = 0.044715


def gelu_fwd(x):
    return 0.5 * x * (1.0 + jnp.tanh(coef * (x + cubic * x * x * x)))


def gelu_grad(x):
    inner = coef * (x + cubic * x * x * x)
    tangent = jnp.tanh(inner)
    return 0.5 * (1.0 + tangent) + 0.5 * x * (1.0 - tangent * tangent) * coef * (
        1.0 + 3.0 * cubic * x * x
    )


def ring_gather(block, axis, n):
    fwd = block
    bwd = block
    got = {0: block}
    for k in range(1, n // 2 + 1):
        fwd = lax.ppermute(fwd, axis, [(i, (i + 1) % n) for i in range(n)])
        got[(n - k) % n] = fwd
        if k < n - k:
            bwd = lax.ppermute(bwd, axis, [(i, (i - 1) % n) for i in range(n)])
            got[k] = bwd
    return [got[k] for k in range(n)]


def shift_pairs(n, s):
    return [(i, (i + s) % n) for i in range(n)]


def make_body(n_x, n_col, n_core):
    def body(grad_out, pre_act, down_weight):
        rc = lax.axis_index("rc")
        c = lax.axis_index("col")
        tok_blk, width = grad_out.shape
        w_partner = lax.ppermute(down_weight, "rc", shift_pairs(n_core, 1))
        w_both = jnp.concatenate([down_weight, w_partner], axis=0)
        abs_x = lax.all_gather(grad_out, "rx", axis=0, tiled=False)
        g_own = lax.all_gather(abs_x, "ry", axis=1, tiled=False)
        rel = ring_gather(pre_act, "col", n_col)
        n_y = g_own.shape[1]
        go = g_own.reshape(-1, width)
        dn2 = (((1,), (1,)), ((), ()))
        p_both = lax.dot_general(go, w_both, dn2, preferred_element_type=jnp.float32)
        p_both = p_both.astype(jnp.bfloat16).reshape(go.shape[0], n_core, -1)
        g_late, rel, p_both = lax.optimization_barrier((g_own, rel, p_both))
        red = lax.psum_scatter(p_both, "col", scatter_dimension=0, tiled=True)
        g_other = lax.ppermute(g_late, "rc", shift_pairs(n_core, 1))
        rel = jnp.stack(rel)
        both = jnp.concatenate([rel, rel], axis=0)
        pre_abs = lax.dynamic_slice_in_dim(both, (n_col - c) % n_col, n_col, 0)
        hidden = gelu_fwd(pre_abs.astype(jnp.float32)).astype(jnp.bfloat16)
        hid = hidden.shape[-1]
        h5 = hidden.reshape(n_x, n_y, n_core, tok_blk, hid)
        h5 = jnp.transpose(h5, (2, 0, 1, 3, 4))
        h_own = lax.dynamic_index_in_dim(h5, rc, 0, keepdims=False).reshape(-1, hid)
        h_other = lax.dynamic_index_in_dim(h5, (rc + 1) % n_core, 0, keepdims=False).reshape(-1, hid)
        gt = g_other.reshape(-1, width)
        dn = (((0,), (0,)), ((), ()))
        gw = lax.dot_general(h_own, go, dn, preferred_element_type=jnp.float32)
        gw = gw + lax.dot_general(h_other, gt, dn, preferred_element_type=jnp.float32)
        grad_weight = gw.astype(jnp.bfloat16)
        sub = pre_act.shape[0] // (tok_blk * n_core)
        grad_weight, red = lax.optimization_barrier((grad_weight, red))
        got = lax.ppermute(red, "rc", shift_pairs(n_core, 1))
        mine = red[:, 0].reshape(sub, 1, tok_blk, hid)
        theirs = got[:, 1].reshape(sub, 1, tok_blk, hid)
        slot = lax.broadcasted_iota(jnp.int32, (sub, n_core, tok_blk, hid), 1)
        gh = jnp.where(slot == rc, mine, theirs).astype(jnp.float32)
        gg = gelu_grad(pre_act.astype(jnp.float32)).reshape(sub, n_core, tok_blk, hid)
        grad_pre = (gh * gg).reshape(pre_act.shape).astype(jnp.bfloat16)
        return (grad_pre, grad_weight)

    return body


def solution(mesh):
    devs = np.asarray(mesh.devices)
    n_row, n_col = devs.shape
    flat = list(devs.flat)
    chips = {tuple(getattr(d, "coords", (i,))) for i, d in enumerate(flat)}
    n_core = max(1, devs.size // len(chips))
    xs = {tuple(getattr(d, "coords", (i,)))[0] for i, d in enumerate(flat)}
    n_x = len(xs)
    split = Mesh(devs.reshape(n_x, n_row // (n_x * n_core), n_core, n_col), ("rx", "ry", "rc", "col"))
    row = ("rx", "ry", "rc")
    in_specs = (P(row, "col"), P("col", row), P(row, "col"))
    out_specs = (P("col", row), P(row, "col"))
    return jax.shard_map(
        make_body(n_x, n_col, n_core), mesh=split, in_specs=in_specs, out_specs=out_specs, check_vma=False
    )
```

```python
import jax
import jax.numpy as jnp
import numpy as np
from jax import lax
from jax.sharding import Mesh
from jax.sharding import PartitionSpec as P

coef = 0.7978845608
cubic = 0.044715


def gelu_fwd(x):
    return 0.5 * x * (1.0 + jnp.tanh(coef * (x + cubic * x * x * x)))


def gelu_grad(x):
    inner = coef * (x + cubic * x * x * x)
    tangent = jnp.tanh(inner)
    return 0.5 * (1.0 + tangent) + 0.5 * x * (1.0 - tangent * tangent) * coef * (
        1.0 + 3.0 * cubic * x * x
    )


def ring_gather(block, axis, n):
    fwd = block
    bwd = block
    got = {0: block}
    for k in range(1, n // 2 + 1):
        fwd = lax.ppermute(fwd, axis, [(i, (i + 1) % n) for i in range(n)])
        got[(n - k) % n] = fwd
        if k < n - k:
            bwd = lax.ppermute(bwd, axis, [(i, (i - 1) % n) for i in range(n)])
            got[k] = bwd
    return [got[k] for k in range(n)]


def shift_pairs(n, s):
    return [(i, (i + s) % n) for i in range(n)]


def make_body(n_x, n_col, n_core):
    def body(grad_out, pre_act, down_weight):
        rc = lax.axis_index("rc")
        c = lax.axis_index("col")
        tok_blk, width = grad_out.shape
        w_partner = lax.ppermute(down_weight, "rc", shift_pairs(n_core, 1))
        w_both = jnp.concatenate([down_weight, w_partner], axis=0)
        copies = jnp.broadcast_to(grad_out[None], (n_x,) + grad_out.shape)
        abs_x = lax.all_to_all(copies, "rx", 0, 0, tiled=False)
        g_own = lax.all_gather(abs_x, "ry", axis=1, tiled=False)
        rel = ring_gather(pre_act, "col", n_col)
        n_y = g_own.shape[1]
        go = g_own.reshape(-1, width)
        dn2 = (((1,), (1,)), ((), ()))
        p_both = lax.dot_general(go, w_both, dn2, preferred_element_type=jnp.float32)
        p_both = p_both.astype(jnp.bfloat16).reshape(go.shape[0], n_core, -1)
        g_late, rel, p_both = lax.optimization_barrier((g_own, rel, p_both))
        red = lax.psum_scatter(p_both, "col", scatter_dimension=0, tiled=True)
        g_other = lax.ppermute(g_late, "rc", shift_pairs(n_core, 1))
        rel = jnp.stack(rel)
        both = jnp.concatenate([rel, rel], axis=0)
        pre_abs = lax.dynamic_slice_in_dim(both, (n_col - c) % n_col, n_col, 0)
        hidden = gelu_fwd(pre_abs.astype(jnp.float32)).astype(jnp.bfloat16)
        hid = hidden.shape[-1]
        h5 = hidden.reshape(n_x, n_y, n_core, tok_blk, hid)
        h5 = jnp.transpose(h5, (2, 0, 1, 3, 4))
        h_own = lax.dynamic_index_in_dim(h5, rc, 0, keepdims=False).reshape(-1, hid)
        h_other = lax.dynamic_index_in_dim(h5, (rc + 1) % n_core, 0, keepdims=False).reshape(-1, hid)
        gt = g_other.reshape(-1, width)
        dn = (((0,), (0,)), ((), ()))
        gw = lax.dot_general(h_own, go, dn, preferred_element_type=jnp.float32)
        gw = gw + lax.dot_general(h_other, gt, dn, preferred_element_type=jnp.float32)
        grad_weight = gw.astype(jnp.bfloat16)
        sub = pre_act.shape[0] // (tok_blk * n_core)
        grad_weight, red = lax.optimization_barrier((grad_weight, red))
        got = lax.ppermute(red, "rc", shift_pairs(n_core, 1))
        mine = red[:, 0].reshape(sub, 1, tok_blk, hid)
        theirs = got[:, 1].reshape(sub, 1, tok_blk, hid)
        slot = lax.broadcasted_iota(jnp.int32, (sub, n_core, tok_blk, hid), 1)
        gh = jnp.where(slot == rc, mine, theirs).astype(jnp.float32)
        gg = gelu_grad(pre_act.astype(jnp.float32)).reshape(sub, n_core, tok_blk, hid)
        grad_pre = (gh * gg).reshape(pre_act.shape).astype(jnp.bfloat16)
        return (grad_pre, grad_weight)

    return body


def solution(mesh):
    devs = np.asarray(mesh.devices)
    n_row, n_col = devs.shape
    flat = list(devs.flat)
    chips = {tuple(getattr(d, "coords", (i,))) for i, d in enumerate(flat)}
    n_core = max(1, devs.size // len(chips))
    xs = {tuple(getattr(d, "coords", (i,)))[0] for i, d in enumerate(flat)}
    n_x = len(xs)
    split = Mesh(devs.reshape(n_x, n_row // (n_x * n_core), n_core, n_col), ("rx", "ry", "rc", "col"))
    row = ("rx", "ry", "rc")
    in_specs = (P(row, "col"), P("col", row), P(row, "col"))
    out_specs = (P("col", row), P(row, "col"))
    return jax.shard_map(
        make_body(n_x, n_col, n_core), mesh=split, in_specs=in_specs, out_specs=out_specs, check_vma=False
    )
```

```python
import jax
import jax.numpy as jnp
import numpy as np
from jax import lax
from jax.sharding import Mesh
from jax.sharding import PartitionSpec as P

coef = 0.7978845608
cubic = 0.044715


def gelu_fwd(x):
    return 0.5 * x * (1.0 + jnp.tanh(coef * (x + cubic * x * x * x)))


def gelu_grad(x):
    inner = coef * (x + cubic * x * x * x)
    tangent = jnp.tanh(inner)
    return 0.5 * (1.0 + tangent) + 0.5 * x * (1.0 - tangent * tangent) * coef * (
        1.0 + 3.0 * cubic * x * x
    )


def ring_gather(block, axis, n):
    fwd = block
    bwd = block
    got = {0: block}
    for k in range(1, n // 2 + 1):
        fwd = lax.ppermute(fwd, axis, [(i, (i + 1) % n) for i in range(n)])
        got[(n - k) % n] = fwd
        if k < n - k:
            bwd = lax.ppermute(bwd, axis, [(i, (i - 1) % n) for i in range(n)])
            got[k] = bwd
    return [got[k] for k in range(n)]


def shift_pairs(n, s):
    return [(i, (i + s) % n) for i in range(n)]


def make_body(n_x, n_col, n_core):
    def body(grad_out, pre_act, down_weight):
        rc = lax.axis_index("rc")
        c = lax.axis_index("col")
        tok_blk, width = grad_out.shape
        w_partner = lax.ppermute(down_weight, "rc", shift_pairs(n_core, 1))
        w_both = jnp.concatenate([down_weight, w_partner], axis=0)
        copies = jnp.broadcast_to(grad_out[None], (n_x,) + grad_out.shape)
        abs_x = lax.all_to_all(copies, "rx", 0, 0, tiled=False)
        g_own = lax.all_gather(abs_x, "ry", axis=1, tiled=False)
        rel = ring_gather(pre_act, "col", n_col)
        n_y = g_own.shape[1]
        go = g_own.reshape(-1, width)
        dn2 = (((1,), (1,)), ((), ()))
        p_both = lax.dot_general(go, w_both, dn2, preferred_element_type=jnp.float32)
        p_both = p_both.astype(jnp.bfloat16).reshape(go.shape[0], n_core, -1)
        g_late, rel, p_both = lax.optimization_barrier((g_own, rel, p_both))
        red = lax.psum_scatter(p_both, "col", scatter_dimension=0, tiled=True)
        g_other = lax.ppermute(g_late, "rc", shift_pairs(n_core, 1))
        rel = jnp.stack(rel)
        both = jnp.concatenate([rel, rel], axis=0)
        pre_abs = lax.dynamic_slice_in_dim(both, (n_col - c) % n_col, n_col, 0)
        hidden = gelu_fwd(pre_abs.astype(jnp.float32)).astype(jnp.bfloat16)
        hid = hidden.shape[-1]
        h5 = hidden.reshape(n_x, n_y, n_core, tok_blk, hid)
        h5 = jnp.transpose(h5, (2, 0, 1, 3, 4))
        h_own = lax.dynamic_index_in_dim(h5, rc, 0, keepdims=False).reshape(-1, hid)
        h_other = lax.dynamic_index_in_dim(h5, (rc + 1) % n_core, 0, keepdims=False).reshape(-1, hid)
        gt = g_other.reshape(-1, width)
        dn = (((0,), (0,)), ((), ()))
        gw = lax.dot_general(h_own, go, dn, preferred_element_type=jnp.float32)
        gw = gw + lax.dot_general(h_other, gt, dn, preferred_element_type=jnp.float32)
        grad_weight = gw.astype(jnp.bfloat16)
        sub = pre_act.shape[0] // (tok_blk * n_core)
        grad_weight, red = lax.optimization_barrier((grad_weight, red))
        send = jnp.where(rc == 0, jnp.stack([red[:, 0], red[:, 1]]), jnp.stack([red[:, 1], red[:, 0]]))
        recv = lax.all_to_all(send, "rc", 0, 0, tiled=False)
        gh = jnp.transpose(recv.reshape(n_core, sub, tok_blk, hid), (1, 0, 2, 3)).astype(jnp.float32)
        gg = gelu_grad(pre_act.astype(jnp.float32)).reshape(sub, n_core, tok_blk, hid)
        grad_pre = (gh * gg).reshape(pre_act.shape).astype(jnp.bfloat16)
        return (grad_pre, grad_weight)

    return body


def solution(mesh):
    devs = np.asarray(mesh.devices)
    n_row, n_col = devs.shape
    flat = list(devs.flat)
    chips = {tuple(getattr(d, "coords", (i,))) for i, d in enumerate(flat)}
    n_core = max(1, devs.size // len(chips))
    xs = {tuple(getattr(d, "coords", (i,)))[0] for i, d in enumerate(flat)}
    n_x = len(xs)
    split = Mesh(devs.reshape(n_x, n_row // (n_x * n_core), n_core, n_col), ("rx", "ry", "rc", "col"))
    row = ("rx", "ry", "rc")
    in_specs = (P(row, "col"), P("col", row), P(row, "col"))
    out_specs = (P("col", row), P(row, "col"))
    return jax.shard_map(
        make_body(n_x, n_col, n_core), mesh=split, in_specs=in_specs, out_specs=out_specs, check_vma=False
    )
```
